256 devices in a mesh: dp: 2 (over core), expert: 128 (over x, z, y).
Axes of the slice: x: 4, y: 4, z: 8, core: 2. Of those that a mesh axis runs over, the one named last changes fastest.
Arguments:
- states: bfloat16 [3, 32768, 1024], P(None, ('dp', 'expert')), may hold values from -6 to 6
- language: int32 [3, 32768, 1], P(None, ('dp', 'expert')), may hold values from 0 to 127; in each aligned block of 128 rows (0 to 127, 128 to 255, ..., all dimensions but the last counted through in order) at most 2 rows name the same one
- placement: int32 [3, 128], replicated, may hold values from 0 to 127, each once within a row
- swap_flags: int32 [128], replicated, may hold values from 0 to 1, as said below
- up_weight: bfloat16 [128, 1024, 4096], P('expert', None, 'dp'), may hold values from -0.1875 to 0.1875
- down_weight: bfloat16 [128, 4096, 1024], P('expert', 'dp'), may hold values from -0.09375 to 0.09375
Outputs:
- updated: bfloat16 [3, 32768, 1024], P(None, ('dp', 'expert'))
The draws below stay inside these ranges and needn't reach their ends.
Inputs may be any that keep to these rules, and one draw needn't show every extreme that they name: In the 128 rows of one device at one step (aligned blocks along the rows), no language id occurs more than 2 times, and some id occurs exactly 2 times. `placement`: each step's row is a permutation of the devices of the expert axis. swap_flags[j] equals swap_flags[j + 64] for j under 128/2.
All inputs are finite; a program needn't handle non-finite values.
Results may differ from the reference program's by a relative error of at most 0.0047.
Values may be sent and summed in bfloat16 or wider, within the bound.
No kernel may reach another device: no remote copies, remote signals or barrier semaphores. Data moves between devices by JAX's collectives and lax.ppermute only.
A program may use at most 128 MiB of HBM per device.

```python
import math
import jax
import jax.numpy as jnp
import numpy as np
from jax import lax

D = 1024
HID = 4096
ROWS_DEV = 128
STEPS = 3
EXPERTS = 128
LANGS = 128
CAP = 2
TOKENS = 32768
N_DP = 2
N_EXPERT = 128


def draw_swap_flags(key, part):
    first_half = jax.random.randint(key, (EXPERTS // 2,), 0, 2, dtype=jnp.int32)
    return jnp.concatenate([first_half, first_half])


def steps_of(key, extent, split, low, largest):
    factor_of, own = 1.0, jax.random.fold_in(key, 6)
    for dim, shards_of in split:
        heights = jnp.exp(jax.random.uniform(jax.random.fold_in(own, dim), (shards_of,), jnp.float32, low / len(split), largest / len(split)))
        factor_of = factor_of * jnp.repeat(heights, extent[dim] // shards_of).reshape([-1 if axis == dim else 1 for axis in range(len(extent))])
    return factor_of


def assign_block(rng, own, number, rows, amount, top, reach, skew):
    order = jax.random.permutation(rng, amount)
    crowded, ordinary = portions_of(amount, rows * top, reach, skew, True), portions_of(amount, rows * top, reach, skew, False)
    places = jnp.arange(amount)

    def named(sizes, rotation):
        used = int((sizes > 0).sum())
        fixed = max(1, used // 4)
        moved = fixed + (places - fixed + rotation * (used - fixed)) % max(1, amount - fixed)
        return jnp.zeros((amount,), jnp.int32).at[order[jnp.where(places < fixed, places, moved)]].set(jnp.asarray(sizes, jnp.int32))

    sizes = jnp.where(number % 4 == 0, named(crowded, number // 4), named(ordinary, number - number // 4 - 1))
    mixed = jax.random.permutation(jax.random.fold_in(own, 3), amount)
    giver, sink = mixed[0:amount // 2 * 2:2], mixed[1:amount // 2 * 2:2]
    slack = jnp.minimum(sizes[giver] - 1, reach - sizes[sink]) // 2
    slack = jnp.where((giver == order[0]) | (sink == order[0]) | (sizes[sink] == 0), 0, jnp.maximum(slack, 0))
    moved = jax.random.randint(jax.random.fold_in(own, 4), (amount // 2,), 0, 1 << 20) % (slack + 1)
    sizes = sizes.at[giver].add(-moved).at[sink].add(moved)
    items = jnp.searchsorted(jnp.cumsum(sizes), jnp.arange(rows * top), side="right").astype(jnp.int32)
    table = items.reshape(top, rows).T
    table = table[jax.random.permutation(jax.random.fold_in(own, 1), rows)]
    rotation = jax.random.randint(jax.random.fold_in(own, 2), (rows, 1), 0, top)
    return jnp.take_along_axis(table, (jnp.arange(top)[None, :] + rotation) % top, axis=1)


def portions_of(number_of, total, most, slope, full):
    portions = [(1 << 20) // math.isqrt(rank ** slope) + 1 for rank in range(1, number_of + 1)]
    largest = most if full else min(most, max(-(-total // number_of), total * portions[0] // sum(portions)))
    least = 1 if total - largest >= number_of - 1 else 0
    holding, spare = [largest] + [least] * (number_of - 1), total - largest - least * (number_of - 1)
    while spare > 0:
        movable = [i for i in range(1, number_of) if holding[i] < largest] or [i for i in range(1, number_of) if holding[i] < most]
        mass, budget = sum([portions[i] for i in movable]), spare
        for i in movable:
            addition = min(most - holding[i], max(1, budget * portions[i] // mass), spare)
            holding[i] = holding[i] + addition
            spare = spare - addition
    return np.array(holding)


def scatter_about(own_key, dims, spread, most, cuts=(), kind=jnp.bfloat16):
    factor_of = steps_of(own_key, dims, cuts, -0.22, 0.18) if cuts else 1.0
    array = jax.random.normal(own_key, dims, jnp.float32) * spread * factor_of
    return jnp.minimum(jnp.maximum(array, -most), most).astype(kind)


def setup_inputs(seed: int = 0) -> dict:
    streams_of = jax.random.split(jax.random.key(seed), 7)
    states = scatter_about(streams_of[0], (STEPS, TOKENS, D), 1.0, 6.0, ((1, 256),))
    language_keys = jax.random.split(jax.random.fold_in(streams_of[1], 1), STEPS * TOKENS // ROWS_DEV)
    language_turns = jax.random.permutation(jax.random.fold_in(streams_of[1], 3), STEPS * TOKENS // ROWS_DEV)
    language = jax.vmap(lambda own, number: assign_block(jax.random.fold_in(streams_of[1], 2), own, number, ROWS_DEV, LANGS, 1, CAP, 2))(language_keys, language_turns).reshape((STEPS, TOKENS, 1))
    placement = jax.vmap(lambda own: jax.random.permutation(own, EXPERTS))(jax.random.split(streams_of[2], STEPS)).reshape((STEPS, LANGS)).astype(jnp.int32)
    swap_flags = draw_swap_flags(jax.random.fold_in(streams_of[6], 71), 0)
    up_weight = scatter_about(streams_of[4], (EXPERTS, D, HID), D ** -0.5, 0.1875, ((0, 128), (2, 2)))
    down_weight = scatter_about(streams_of[5], (EXPERTS, HID, D), HID ** -0.5, 0.09375, ((0, 128), (1, 2)))
    return dict(states=states, language=language, placement=placement, swap_flags=swap_flags, up_weight=up_weight, down_weight=down_weight)


def feed_forward(row_block, up_matrix, down_matrix):
    hidden = jnp.maximum(jnp.dot(row_block, up_matrix, preferred_element_type=jnp.float32), 0.0).astype(jnp.bfloat16)
    return jnp.dot(hidden, down_matrix, preferred_element_type=jnp.float32).astype(jnp.bfloat16)


def serve_rows(row_states, served, up_weight, down_weight):
    labels = jnp.arange(EXPERTS, dtype=jnp.int32)
    counts = jnp.sum((served[:, None] == labels[None, :]).astype(jnp.int32), axis=0).astype(jnp.int32)
    starts = (jnp.cumsum(counts) - counts).astype(jnp.int32)
    row_order = jnp.argsort(served, stable=True).astype(jnp.int32)
    sorted_rows = row_states[row_order]
    offsets = jnp.arange(CAP * N_DP * N_EXPERT, dtype=jnp.int32)

    def one_expert(running, expert):
        positions = jnp.minimum(starts[expert] + offsets, TOKENS - 1).astype(jnp.int32)
        is_filled = offsets < counts[expert]
        row_block = sorted_rows[positions]
        up_matrix = lax.dynamic_index_in_dim(up_weight, expert, 0, keepdims=False)
        down_matrix = lax.dynamic_index_in_dim(down_weight, expert, 0, keepdims=False)
        expert_out = feed_forward(row_block, up_matrix, down_matrix).astype(jnp.float32)
        running = running.at[positions].add(jnp.where(is_filled[:, None], expert_out, jnp.zeros_like(expert_out)))
        return running, None

    zero_rows = jnp.zeros((TOKENS, D), jnp.float32)
    gathered_sum, unused = lax.scan(one_expert, zero_rows, labels)
    return jnp.zeros((TOKENS, D), jnp.float32).at[row_order].set(gathered_sum)


def reference(states, language, placement, swap_flags, up_weight, down_weight):
    labels = jnp.arange(EXPERTS, dtype=jnp.int32)
    resident = jnp.where(swap_flags == 1, (labels + EXPERTS // 2) % EXPERTS, labels).astype(jnp.int32)
    outputs = []
    for step_index in range(STEPS):
        served = placement[step_index][language[step_index, :, 0]].astype(jnp.int32)
        if step_index >= 1:
            served = resident[served].astype(jnp.int32)
        update = serve_rows(states[step_index], served, up_weight, down_weight)
        outputs.append((states[step_index].astype(jnp.float32) + update).astype(jnp.bfloat16))
    return jnp.stack(outputs)
```

```python
import jax
import jax.numpy as jnp
from jax import lax
from jax.sharding import PartitionSpec as P


def make_expert(up_matrix, down_matrix):

    def apply_rows(shard_rows):
        hidden = jnp.maximum(
            jnp.dot(shard_rows, up_matrix, preferred_element_type=jnp.float32), 0.0
        ).astype(jnp.bfloat16)
        return jnp.dot(hidden, down_matrix, preferred_element_type=jnp.float32)

    def expert_fn(arrived):
        source_count, slot_count, model_width = arrived.shape
        flat_rows = arrived.reshape(source_count * slot_count, model_width)
        partial_terms = apply_rows(lax.all_gather(flat_rows, "dp", axis=0, tiled=True))
        own_share = lax.psum_scatter(partial_terms, "dp", scatter_dimension=0, tiled=True)
        return own_share.astype(jnp.bfloat16).reshape(source_count, slot_count, model_width)

    return expert_fn


def shards(states, language, placement, swap_flags, up_weight, down_weight):
    step_count, row_count, model_width = states.shape
    experts = lax.axis_size("expert")
    capacity = max(2, 2 * row_count // experts)
    labels = jnp.arange(experts, dtype=jnp.int32)
    resident = jnp.where(swap_flags == 1, (labels + experts // 2) % experts, labels)
    expert_fn = make_expert(up_weight[0], down_weight[0])
    slot_labels = jnp.arange(experts * capacity, dtype=jnp.int32)
    outputs = []
    for step_index in range(step_count):
        route = placement[step_index]
        if step_index >= 1:
            route_hot = (route[:, None] == labels[None, :]).astype(jnp.int32)
            route = jnp.sum(route_hot * resident[None, :], axis=1)
        lang_hot = (language[step_index, :, 0][:, None] == labels[None, :]).astype(jnp.int32)
        target = jnp.sum(lang_hot * route[None, :], axis=1)
        dest_hot = (target[:, None] == labels[None, :]).astype(jnp.int32)
        earlier = jnp.cumsum(dest_hot, axis=0) - dest_hot
        position_in = jnp.sum(earlier * dest_hot, axis=1)
        slot_index = target * capacity + position_in
        select = (slot_index[:, None] == slot_labels[None, :]).astype(jnp.bfloat16)
        outgoing = jnp.einsum(
            "rs,rd->sd", select, states[step_index], preferred_element_type=jnp.float32
        )
        outgoing = outgoing.astype(jnp.bfloat16).reshape(experts, capacity, model_width)
        served = expert_fn(
            lax.all_to_all(outgoing, "expert", split_axis=0, concat_axis=0, tiled=True)
        )
        returned = lax.all_to_all(served, "expert", split_axis=0, concat_axis=0, tiled=True)
        selected = jnp.dot(
            select,
            returned.reshape(experts * capacity, model_width),
            preferred_element_type=jnp.float32,
        )
        outputs.append((states[step_index].astype(jnp.float32) + selected).astype(jnp.bfloat16))
    return jnp.stack(outputs)


def solution(mesh):
    placed = (
        P(None, ("dp", "expert"), None),
        P(None, ("dp", "expert"), None),
        P(),
        P(),
        P("expert", None, "dp"),
        P("expert", "dp", None),
    )
    return jax.shard_map(
        shards,
        mesh=mesh,
        in_specs=placed,
        out_specs=P(None, ("dp", "expert"), None),
        check_vma=False,
    )
```

```python
import jax
import jax.numpy as jnp
from jax import lax
from jax.sharding import PartitionSpec as P


def shards(states, language, placement, swap_flags, up_weight, down_weight):
    step_count, row_count, model_width = states.shape
    experts = lax.axis_size("expert")
    capacity = max(2, 2 * row_count // experts)
    labels = jnp.arange(experts, dtype=jnp.int32)
    resident = jnp.where(swap_flags == 1, (labels + experts // 2) % experts, labels)
    slot_labels = jnp.arange(experts * capacity, dtype=jnp.int32)
    selects = []
    outgoing = []
    for step_index in range(step_count):
        route = placement[step_index]
        if step_index >= 1:
            route_hot = (route[:, None] == labels[None, :]).astype(jnp.int32)
            route = jnp.sum(route_hot * resident[None, :], axis=1)
        lang_hot = (language[step_index, :, 0][:, None] == labels[None, :]).astype(jnp.int32)
        target = jnp.sum(lang_hot * route[None, :], axis=1)
        dest_hot = (target[:, None] == labels[None, :]).astype(jnp.int32)
        earlier = jnp.cumsum(dest_hot, axis=0) - dest_hot
        position_in = jnp.sum(earlier * dest_hot, axis=1)
        slot_index = target * capacity + position_in
        select = (slot_index[:, None] == slot_labels[None, :]).astype(jnp.bfloat16)
        selects.append(select)
        sent = jnp.einsum(
            "rs,rd->sd", select, states[step_index], preferred_element_type=jnp.float32
        )
        outgoing.append(sent.astype(jnp.bfloat16).reshape(experts, capacity, model_width))
    outgoing = jnp.concatenate(outgoing, axis=1)
    arrived = lax.all_to_all(outgoing, "expert", split_axis=0, concat_axis=0, tiled=True)
    slot_count = step_count * capacity
    flat_rows = arrived.reshape(experts * slot_count, model_width)
    both_halves = lax.all_gather(flat_rows, "dp", axis=0, tiled=True)
    hidden = jnp.maximum(
        jnp.dot(both_halves, up_weight[0], preferred_element_type=jnp.float32), 0.0
    ).astype(jnp.bfloat16)
    partial_terms = jnp.dot(hidden, down_weight[0], preferred_element_type=jnp.float32)
    own_share = lax.psum_scatter(partial_terms, "dp", scatter_dimension=0, tiled=True)
    served = own_share.astype(jnp.bfloat16).reshape(experts, slot_count, model_width)
    returned = lax.all_to_all(served, "expert", split_axis=0, concat_axis=0, tiled=True)
    outputs = []
    for step_index in range(step_count):
        back = returned[:, step_index * capacity:(step_index + 1) * capacity]
        selected = jnp.dot(
            selects[step_index],
            back.reshape(experts * capacity, model_width),
            preferred_element_type=jnp.float32,
        )
        outputs.append((states[step_index].astype(jnp.float32) + selected).astype(jnp.bfloat16))
    return jnp.stack(outputs)


def solution(mesh):
    placed = (
        P(None, ("dp", "expert"), None),
        P(None, ("dp", "expert"), None),
        P(),
        P(),
        P("expert", None, "dp"),
        P("expert", "dp", None),
    )
    return jax.shard_map(
        shards,
        mesh=mesh,
        in_specs=placed,
        out_specs=P(None, ("dp", "expert"), None),
        check_vma=False,
    )
```

```python
import jax
import jax.numpy as jnp
from jax import lax
from jax.sharding import PartitionSpec as P


def shards(states, language, placement, swap_flags, up_weight, down_weight):
    step_count, row_count, model_width = states.shape
    experts = lax.axis_size("expert")
    capacity = max(2, 2 * row_count // experts)
    labels = jnp.arange(experts, dtype=jnp.int32)
    resident = jnp.where(swap_flags == 1, (labels + experts // 2) % experts, labels)
    pair = [(0, 1), (1, 0)]
    other_up = lax.ppermute(up_weight[0], "dp", pair)
    other_down = lax.ppermute(down_weight[0], "dp", pair)
    first = lax.axis_index("dp") == 0
    up_full = jnp.where(first, jnp.concatenate([up_weight[0], other_up], axis=1),
                        jnp.concatenate([other_up, up_weight[0]], axis=1))
    down_full = jnp.where(first, jnp.concatenate([down_weight[0], other_down], axis=0),
                          jnp.concatenate([other_down, down_weight[0]], axis=0))
    slot_labels = jnp.arange(experts * capacity, dtype=jnp.int32)
    selects = []
    outgoing = []
    for step_index in range(step_count):
        route = placement[step_index]
        if step_index >= 1:
            route_hot = (route[:, None] == labels[None, :]).astype(jnp.int32)
            route = jnp.sum(route_hot * resident[None, :], axis=1)
        lang_hot = (language[step_index, :, 0][:, None] == labels[None, :]).astype(jnp.int32)
        target = jnp.sum(lang_hot * route[None, :], axis=1)
        dest_hot = (target[:, None] == labels[None, :]).astype(jnp.int32)
        earlier = jnp.cumsum(dest_hot, axis=0) - dest_hot
        position_in = jnp.sum(earlier * dest_hot, axis=1)
        slot_index = target * capacity + position_in
        select = (slot_index[:, None] == slot_labels[None, :]).astype(jnp.bfloat16)
        selects.append(select)
        sent = jnp.einsum(
            "rs,rd->sd", select, states[step_index], preferred_element_type=jnp.float32
        )
        outgoing.append(sent.astype(jnp.bfloat16).reshape(experts, capacity, model_width))
    outgoing = jnp.concatenate(outgoing, axis=1)
    arrived = lax.all_to_all(outgoing, "expert", split_axis=0, concat_axis=0, tiled=True)
    slot_count = step_count * capacity
    flat_rows = arrived.reshape(experts * slot_count, model_width)
    hidden = jnp.maximum(
        jnp.dot(flat_rows, up_full, preferred_element_type=jnp.float32), 0.0
    ).astype(jnp.bfloat16)
    update = jnp.dot(hidden, down_full, preferred_element_type=jnp.float32)
    served = update.astype(jnp.bfloat16).reshape(experts, slot_count, model_width)
    returned = lax.all_to_all(served, "expert", split_axis=0, concat_axis=0, tiled=True)
    outputs = []
    for step_index in range(step_count):
        back = returned[:, step_index * capacity:(step_index + 1) * capacity]
        selected = jnp.dot(
            selects[step_index],
            back.reshape(experts * capacity, model_width),
            preferred_element_type=jnp.float32,
        )
        outputs.append((states[step_index].astype(jnp.float32) + selected).astype(jnp.bfloat16))
    return jnp.stack(outputs)


def solution(mesh):
    placed = (
        P(None, ("dp", "expert"), None),
        P(None, ("dp", "expert"), None),
        P(),
        P(),
        P("expert", None, "dp"),
        P("expert", "dp", None),
    )
    return jax.shard_map(
        shards,
        mesh=mesh,
        in_specs=placed,
        out_specs=P(None, ("dp", "expert"), None),
        check_vma=False,
    )
```

```python
import jax
import jax.numpy as jnp
from jax import lax
from jax.sharding import PartitionSpec as P


def shards(states, language, placement, swap_flags, up_weight, down_weight):
    step_count, row_count, model_width = states.shape
    experts = lax.axis_size("expert")
    capacity = max(2, 2 * row_count // experts)
    labels = jnp.arange(experts, dtype=jnp.int32)
    pair = [(0, 1), (1, 0)]
    other_up = lax.ppermute(up_weight[0], "dp", pair)
    other_down = lax.ppermute(down_weight[0], "dp", pair)
    first = lax.axis_index("dp") == 0
    up_full = jnp.where(first, jnp.concatenate([up_weight[0], other_up], axis=1),
                        jnp.concatenate([other_up, up_weight[0]], axis=1))
    down_full = jnp.where(first, jnp.concatenate([down_weight[0], other_down], axis=0),
                          jnp.concatenate([other_down, down_weight[0]], axis=0))
    resident = jnp.where(swap_flags == 1, (labels + experts // 2) % experts, labels)
    slots_per = step_count * capacity
    slot_ids = []
    for step_index in range(step_count):
        route = placement[step_index]
        if step_index >= 1:
            route_hot = (route[:, None] == labels[None, :]).astype(jnp.int32)
            route = jnp.sum(route_hot * resident[None, :], axis=1)
        lang_hot = (language[step_index, :, 0][:, None] == labels[None, :]).astype(jnp.int32)
        target = jnp.sum(lang_hot * route[None, :], axis=1)
        dest_hot = (target[:, None] == labels[None, :]).astype(jnp.int32)
        earlier = jnp.cumsum(dest_hot, axis=0) - dest_hot
        position_in = jnp.sum(earlier * dest_hot, axis=1)
        slot_ids.append(target * slots_per + step_index * capacity + position_in)
    slot_id = jnp.concatenate(slot_ids)
    slot_labels = jnp.arange(experts * slots_per, dtype=jnp.int32)
    select = (slot_id[:, None] == slot_labels[None, :]).astype(jnp.bfloat16)
    rows = states.reshape(step_count * row_count, model_width)
    outgoing = jnp.einsum("rs,rd->sd", select, rows, preferred_element_type=jnp.float32)
    lanes = 128 if model_width % 128 == 0 else model_width
    packed = (experts, slots_per * model_width // lanes, lanes)
    outgoing = outgoing.astype(jnp.bfloat16).reshape(packed)
    arrived = lax.all_to_all(outgoing, "expert", split_axis=0, concat_axis=0, tiled=True)
    flat_rows = arrived.reshape(experts * slots_per, model_width)
    hidden = jnp.maximum(
        jnp.dot(flat_rows, up_full, preferred_element_type=jnp.float32), 0.0
    ).astype(jnp.bfloat16)
    update = jnp.dot(hidden, down_full, preferred_element_type=jnp.float32)
    served = update.astype(jnp.bfloat16).reshape(packed)
    returned = lax.all_to_all(served, "expert", split_axis=0, concat_axis=0, tiled=True)
    selected = jnp.dot(
        select,
        returned.reshape(experts * slots_per, model_width),
        preferred_element_type=jnp.float32,
    )
    updated = (rows.astype(jnp.float32) + selected).astype(jnp.bfloat16)
    return updated.reshape(step_count, row_count, model_width)


def solution(mesh):
    placed = (
        P(None, ("dp", "expert"), None),
        P(None, ("dp", "expert"), None),
        P(),
        P(),
        P("expert", None, "dp"),
        P("expert", "dp", None),
    )
    return jax.shard_map(
        shards,
        mesh=mesh,
        in_specs=placed,
        out_specs=P(None, ("dp", "expert"), None),
        check_vma=False,
    )
```

```python
import jax
import jax.numpy as jnp
from jax import lax
from jax.sharding import PartitionSpec as P


def shards(states, language, placement, swap_flags, up_weight, down_weight):
    step_count, row_count, model_width = states.shape
    experts = lax.axis_size("expert")
    capacity = max(2, 2 * row_count // experts)
    labels = jnp.arange(experts, dtype=jnp.int32)
    pair = [(0, 1), (1, 0)]
    other_up = lax.ppermute(up_weight[0], "dp", pair)
    other_down = lax.ppermute(down_weight[0], "dp", pair)
    first = lax.axis_index("dp") == 0
    up_full = jnp.where(first, jnp.concatenate([up_weight[0], other_up], axis=1),
                        jnp.concatenate([other_up, up_weight[0]], axis=1))
    down_full = jnp.where(first, jnp.concatenate([down_weight[0], other_down], axis=0),
                          jnp.concatenate([other_down, down_weight[0]], axis=0))
    resident = jnp.where(swap_flags == 1, (labels + experts // 2) % experts, labels)
    slots_per = step_count * capacity
    steps = jnp.arange(step_count, dtype=jnp.int32)
    placed_hot = placement[:, :, None] == labels[None, None, :]
    moved = jnp.sum(jnp.where(placed_hot, resident[None, None, :], 0), axis=2)
    route = jnp.where(steps[:, None] == 0, placement, moved)
    lang_hot = language[:, :, 0][:, :, None] == labels[None, None, :]
    target = jnp.sum(jnp.where(lang_hot, route[:, None, :], 0), axis=2)
    row_ids = jnp.arange(row_count, dtype=jnp.int32)
    same = (target[:, :, None] == target[:, None, :]) & (row_ids[None, None, :] < row_ids[None, :, None])
    position_in = jnp.sum(same.astype(jnp.int32), axis=2)
    slot_id = (target * slots_per + steps[:, None] * capacity + position_in).reshape(-1)
    slot_labels = jnp.arange(experts * slots_per, dtype=jnp.int32)
    select = (slot_id[:, None] == slot_labels[None, :]).astype(jnp.bfloat16)
    rows = states.reshape(step_count * row_count, model_width)
    outgoing = jnp.einsum("rs,rd->sd", select, rows, preferred_element_type=jnp.float32)
    lanes = 128 if model_width % 128 == 0 else model_width
    packed = (experts, slots_per * model_width // lanes, lanes)
    outgoing = outgoing.astype(jnp.bfloat16).reshape(packed)
    arrived = lax.all_to_all(outgoing, "expert", split_axis=0, concat_axis=0, tiled=True)
    flat_rows = arrived.reshape(experts * slots_per, model_width)
    hidden = jnp.maximum(
        jnp.dot(flat_rows, up_full, preferred_element_type=jnp.float32), 0.0
    ).astype(jnp.bfloat16)
    update = jnp.dot(hidden, down_full, preferred_element_type=jnp.float32)
    served = update.astype(jnp.bfloat16).reshape(packed)
    returned = lax.all_to_all(served, "expert", split_axis=0, concat_axis=0, tiled=True)
    selected = jnp.dot(
        select,
        returned.reshape(experts * slots_per, model_width),
        preferred_element_type=jnp.float32,
    )
    updated = (rows.astype(jnp.float32) + selected).astype(jnp.bfloat16)
    return updated.reshape(step_count, row_count, model_width)


def solution(mesh):
    placed = (
        P(None, ("dp", "expert"), None),
        P(None, ("dp", "expert"), None),
        P(),
        P(),
        P("expert", None, "dp"),
        P("expert", "dp", None),
    )
    return jax.shard_map(
        shards,
        mesh=mesh,
        in_specs=placed,
        out_specs=P(None, ("dp", "expert"), None),
        check_vma=False,
    )
```

```python
import jax
import jax.numpy as jnp
from jax import lax
from jax.sharding import PartitionSpec as P


def shards(states, language, placement, swap_flags, up_weight, down_weight):
    step_count, row_count, model_width = states.shape
    experts = lax.axis_size("expert")
    capacity = max(2, 2 * row_count // experts)
    labels = jnp.arange(experts, dtype=jnp.int32)
    pair = [(0, 1), (1, 0)]
    other_up = lax.ppermute(up_weight[0], "dp", pair)
    other_down = lax.ppermute(down_weight[0], "dp", pair)
    up_full = jnp.concatenate([up_weight[0], other_up], axis=1)
    down_full = jnp.concatenate([down_weight[0], other_down], axis=0)
    resident = jnp.where(swap_flags == 1, (labels + experts // 2) % experts, labels)
    slots_per = step_count * capacity
    steps = jnp.arange(step_count, dtype=jnp.int32)
    placed_hot = placement[:, :, None] == labels[None, None, :]
    moved = jnp.sum(jnp.where(placed_hot, resident[None, None, :], 0), axis=2)
    route = jnp.where(steps[:, None] == 0, placement, moved)
    lang_hot = language[:, :, 0][:, :, None] == labels[None, None, :]
    target = jnp.sum(jnp.where(lang_hot, route[:, None, :], 0), axis=2)
    row_ids = jnp.arange(row_count, dtype=jnp.int32)
    same = (target[:, :, None] == target[:, None, :]) & (row_ids[None, None, :] < row_ids[None, :, None])
    position_in = jnp.sum(same.astype(jnp.int32), axis=2)
    slot_id = (target * slots_per + steps[:, None] * capacity + position_in).reshape(-1)
    slot_labels = jnp.arange(experts * slots_per, dtype=jnp.int32)
    select = (slot_id[:, None] == slot_labels[None, :]).astype(jnp.bfloat16)
    rows = states.reshape(step_count * row_count, model_width)
    outgoing = jnp.einsum("rs,rd->sd", select, rows, preferred_element_type=jnp.float32)
    lanes = 128 if model_width % 128 == 0 else model_width
    packed = (experts, slots_per * model_width // lanes, lanes)
    outgoing = outgoing.astype(jnp.bfloat16).reshape(packed)
    arrived = lax.all_to_all(outgoing, "expert", split_axis=0, concat_axis=0, tiled=True)
    flat_rows = arrived.reshape(experts * slots_per, model_width)
    hidden = jnp.maximum(
        jnp.dot(flat_rows, up_full, preferred_element_type=jnp.float32), 0.0
    ).astype(jnp.bfloat16)
    update = jnp.dot(hidden, down_full, preferred_element_type=jnp.float32)
    served = update.astype(jnp.bfloat16).reshape(packed)
    returned = lax.all_to_all(served, "expert", split_axis=0, concat_axis=0, tiled=True)
    selected = jnp.dot(
        select,
        returned.reshape(experts * slots_per, model_width),
        preferred_element_type=jnp.float32,
    )
    updated = (rows.astype(jnp.float32) + selected).astype(jnp.bfloat16)
    return updated.reshape(step_count, row_count, model_width)


def solution(mesh):
    placed = (
        P(None, ("dp", "expert"), None),
        P(None, ("dp", "expert"), None),
        P(),
        P(),
        P("expert", None, "dp"),
        P("expert", "dp", None),
    )
    return jax.shard_map(
        shards,
        mesh=mesh,
        in_specs=placed,
        out_specs=P(None, ("dp", "expert"), None),
        check_vma=False,
    )
```

```python
import jax
import jax.numpy as jnp
from jax import lax
from jax.experimental import pallas as pl
from jax.experimental.pallas import tpu as pltpu
from jax.sharding import PartitionSpec as P


def expert_ffn(rows, up_own, up_other, down_own, down_other, interpret=False):
    row_count, model_width = rows.shape
    half = up_own.shape[1]
    block = 512 if half % 512 == 0 else half
    blocks = half // block

    def kernel(x_ref, ua_ref, ub_ref, da_ref, db_ref, o_ref, acc_ref):
        side = pl.program_id(0)
        chunk = pl.program_id(1)

        @pl.when((side == 0) & (chunk == 0))
        def _():
            acc_ref[...] = jnp.zeros_like(acc_ref)

        def accumulate(u_ref, d_ref):
            hidden = jnp.maximum(
                jnp.dot(x_ref[...], u_ref[...], preferred_element_type=jnp.float32), 0.0
            ).astype(jnp.bfloat16)
            acc_ref[...] += jnp.dot(hidden, d_ref[...], preferred_element_type=jnp.float32)

        @pl.when(side == 0)
        def _():
            accumulate(ua_ref, da_ref)

        @pl.when(side == 1)
        def _():
            accumulate(ub_ref, db_ref)

        @pl.when((side == 1) & (chunk == blocks - 1))
        def _():
            o_ref[...] = acc_ref[...].astype(o_ref.dtype)

    def own(side, chunk):
        return chunk * (1 - side) + (blocks - 1) * side

    def other(side, chunk):
        return chunk * side

    return pl.pallas_call(
        kernel,
        out_shape=jax.ShapeDtypeStruct((row_count, model_width), jnp.bfloat16),
        grid=(2, blocks),
        in_specs=[
            pl.BlockSpec((row_count, model_width), lambda s, c: (0, 0)),
            pl.BlockSpec((model_width, block), lambda s, c: (0, own(s, c))),
            pl.BlockSpec((model_width, block), lambda s, c: (0, other(s, c))),
            pl.BlockSpec((block, model_width), lambda s, c: (own(s, c), 0)),
            pl.BlockSpec((block, model_width), lambda s, c: (other(s, c), 0)),
        ],
        out_specs=pl.BlockSpec((row_count, model_width), lambda s, c: (0, 0)),
        scratch_shapes=[pltpu.VMEM((row_count, model_width), jnp.float32)],
        interpret=interpret,
    )(rows, up_own, up_other, down_own, down_other)


def shards(states, language, placement, swap_flags, up_weight, down_weight):
    step_count, row_count, model_width = states.shape
    experts = lax.axis_size("expert")
    capacity = max(2, 2 * row_count // experts)
    labels = jnp.arange(experts, dtype=jnp.int32)
    pair = [(0, 1), (1, 0)]
    other_up = lax.ppermute(up_weight[0], "dp", pair)
    other_down = lax.ppermute(down_weight[0], "dp", pair)
    resident = jnp.where(swap_flags == 1, (labels + experts // 2) % experts, labels)
    slots_per = step_count * capacity
    steps = jnp.arange(step_count, dtype=jnp.int32)
    placed_hot = placement[:, :, None] == labels[None, None, :]
    moved = jnp.sum(jnp.where(placed_hot, resident[None, None, :], 0), axis=2)
    route = jnp.where(steps[:, None] == 0, placement, moved)
    lang_hot = language[:, :, 0][:, :, None] == labels[None, None, :]
    target = jnp.sum(jnp.where(lang_hot, route[:, None, :], 0), axis=2)
    row_ids = jnp.arange(row_count, dtype=jnp.int32)
    same = (target[:, :, None] == target[:, None, :]) & (row_ids[None, None, :] < row_ids[None, :, None])
    position_in = jnp.sum(same.astype(jnp.int32), axis=2)
    slot_id = (target * slots_per + steps[:, None] * capacity + position_in).reshape(-1)
    slot_labels = jnp.arange(experts * slots_per, dtype=jnp.int32)
    select = (slot_id[:, None] == slot_labels[None, :]).astype(jnp.bfloat16)
    rows = states.reshape(step_count * row_count, model_width)
    outgoing = jnp.einsum("rs,rd->sd", select, rows, preferred_element_type=jnp.float32)
    lanes = 128 if model_width % 128 == 0 else model_width
    packed = (experts, slots_per * model_width // lanes, lanes)
    outgoing = outgoing.astype(jnp.bfloat16).reshape(packed)
    arrived = lax.all_to_all(outgoing, "expert", split_axis=0, concat_axis=0, tiled=True)
    flat_rows = arrived.reshape(experts * slots_per, model_width)
    update = expert_ffn(flat_rows, up_weight[0], other_up, down_weight[0], other_down)
    served = update.reshape(packed)
    returned = lax.all_to_all(served, "expert", split_axis=0, concat_axis=0, tiled=True)
    selected = jnp.dot(
        select,
        returned.reshape(experts * slots_per, model_width),
        preferred_element_type=jnp.float32,
    )
    updated = (rows.astype(jnp.float32) + selected).astype(jnp.bfloat16)
    return updated.reshape(step_count, row_count, model_width)


def solution(mesh):
    placed = (
        P(None, ("dp", "expert"), None),
        P(None, ("dp", "expert"), None),
        P(),
        P(),
        P("expert", None, "dp"),
        P("expert", "dp", None),
    )
    return jax.shard_map(
        shards,
        mesh=mesh,
        in_specs=placed,
        out_specs=P(None, ("dp", "expert"), None),
        check_vma=False,
    )
```

```python
import jax
import jax.numpy as jnp
from jax import lax
from jax.sharding import PartitionSpec as P


def shards(states, language, placement, swap_flags, up_weight, down_weight):
    step_count, row_count, model_width = states.shape
    experts = lax.axis_size("expert")
    capacity = max(2, 2 * row_count // experts)
    labels = jnp.arange(experts, dtype=jnp.int32)
    pair = [(0, 1), (1, 0)]
    other_up = lax.ppermute(up_weight[0], "dp", pair)
    other_down = lax.ppermute(down_weight[0], "dp", pair)
    up_full = jnp.concatenate([up_weight[0], other_up], axis=1)
    down_full = jnp.concatenate([down_weight[0], other_down], axis=0)
    resident = jnp.where(swap_flags == 1, (labels + experts // 2) % experts, labels)
    slots_per = step_count * capacity
    steps = jnp.arange(step_count, dtype=jnp.int32)
    placed_hot = placement[:, :, None] == labels[None, None, :]
    moved = jnp.sum(jnp.where(placed_hot, resident[None, None, :], 0), axis=2)
    route = jnp.where(steps[:, None] == 0, placement, moved)
    lang_hot = language[:, :, 0][:, :, None] == labels[None, None, :]
    target = jnp.sum(jnp.where(lang_hot, route[:, None, :], 0), axis=2)
    row_ids = jnp.arange(row_count, dtype=jnp.int32)
    same = (target[:, :, None] == target[:, None, :]) & (row_ids[None, None, :] < row_ids[None, :, None])
    position_in = jnp.sum(same.astype(jnp.int32), axis=2)
    slot_id = (target * slots_per + steps[:, None] * capacity + position_in).reshape(-1)
    slot_labels = jnp.arange(experts * slots_per, dtype=jnp.int32)
    select = (slot_id[:, None] == slot_labels[None, :]).astype(jnp.bfloat16)
    rows = states.reshape(step_count * row_count, model_width)
    outgoing = jnp.einsum("rs,rd->sd", select, rows, preferred_element_type=jnp.float32)
    lanes = 128 if model_width % 128 == 0 else model_width
    packed = (experts, slots_per * model_width // lanes, lanes)
    outgoing = outgoing.astype(jnp.bfloat16).reshape(packed)
    arrived = lax.all_to_all(outgoing, "expert", split_axis=0, concat_axis=0, tiled=True)
    flat_rows = arrived.reshape(experts * slots_per, model_width)
    hidden = jnp.maximum(
        jnp.dot(flat_rows, up_full, preferred_element_type=jnp.float32), 0.0
    ).astype(jnp.bfloat16)
    update = jnp.dot(hidden, down_full, preferred_element_type=jnp.float32)
    served = update.astype(jnp.bfloat16).reshape(packed)
    returned = lax.all_to_all(served, "expert", split_axis=0, concat_axis=0, tiled=True)
    selected = jnp.take(returned.reshape(experts * slots_per, model_width), slot_id, axis=0)
    updated = (rows.astype(jnp.float32) + selected).astype(jnp.bfloat16)
    return updated.reshape(step_count, row_count, model_width)


def solution(mesh):
    placed = (
        P(None, ("dp", "expert"), None),
        P(None, ("dp", "expert"), None),
        P(),
        P(),
        P("expert", None, "dp"),
        P("expert", "dp", None),
    )
    return jax.shard_map(
        shards,
        mesh=mesh,
        in_specs=placed,
        out_specs=P(None, ("dp", "expert"), None),
        check_vma=False,
    )
```

```python
import jax
import jax.numpy as jnp
from jax import lax
from jax.sharding import PartitionSpec as P


def shards(states, language, placement, swap_flags, up_weight, down_weight):
    step_count, row_count, model_width = states.shape
    experts = lax.axis_size("expert")
    capacity = max(2, 2 * row_count // experts)
    labels = jnp.arange(experts, dtype=jnp.int32)
    pair = [(0, 1), (1, 0)]
    other_up = lax.ppermute(up_weight[0], "dp", pair)
    other_down = lax.ppermute(down_weight[0], "dp", pair)
    up_full = jnp.concatenate([up_weight[0], other_up], axis=1)
    down_full = jnp.concatenate([down_weight[0], other_down], axis=0)
    slots_per = step_count * capacity
    steps = jnp.arange(step_count, dtype=jnp.int32)
    placed_hot = placement[:, :, None] == labels[None, None, :]
    flag_at = jnp.sum(jnp.where(placed_hot, swap_flags[None, None, :], 0), axis=2)
    swapped = (steps[:, None] >= 1) & (flag_at == 1)
    route = jnp.where(swapped, (placement + experts // 2) % experts, placement)
    lang_hot = language[:, :, 0][:, :, None] == labels[None, None, :]
    target = jnp.sum(jnp.where(lang_hot, route[:, None, :], 0), axis=2)
    row_ids = jnp.arange(row_count, dtype=jnp.int32)
    same = (target[:, :, None] == target[:, None, :]) & (row_ids[None, None, :] < row_ids[None, :, None])
    position_in = jnp.sum(same.astype(jnp.int32), axis=2)
    slot_id = (target * slots_per + steps[:, None] * capacity + position_in).reshape(-1)
    slot_labels = jnp.arange(experts * slots_per, dtype=jnp.int32)
    select = (slot_id[:, None] == slot_labels[None, :]).astype(jnp.bfloat16)
    rows = states.reshape(step_count * row_count, model_width)
    outgoing = jnp.einsum("rs,rd->sd", select, rows, preferred_element_type=jnp.float32)
    lanes = 128 if model_width % 128 == 0 else model_width
    packed = (experts, slots_per * model_width // lanes, lanes)
    outgoing = outgoing.astype(jnp.bfloat16).reshape(packed)
    arrived = lax.all_to_all(outgoing, "expert", split_axis=0, concat_axis=0, tiled=True)
    flat_rows = arrived.reshape(experts * slots_per, model_width)
    hidden = jnp.maximum(
        jnp.dot(flat_rows, up_full, preferred_element_type=jnp.float32), 0.0
    ).astype(jnp.bfloat16)
    update = jnp.dot(hidden, down_full, preferred_element_type=jnp.float32)
    served = update.astype(jnp.bfloat16).reshape(packed)
    returned = lax.all_to_all(served, "expert", split_axis=0, concat_axis=0, tiled=True)
    selected = jnp.dot(
        select,
        returned.reshape(experts * slots_per, model_width),
        preferred_element_type=jnp.float32,
    )
    updated = (rows.astype(jnp.float32) + selected).astype(jnp.bfloat16)
    return updated.reshape(step_count, row_count, model_width)


def solution(mesh):
    placed = (
        P(None, ("dp", "expert"), None),
        P(None, ("dp", "expert"), None),
        P(),
        P(),
        P("expert", None, "dp"),
        P("expert", "dp", None),
    )
    return jax.shard_map(
        shards,
        mesh=mesh,
        in_specs=placed,
        out_specs=P(None, ("dp", "expert"), None),
        check_vma=False,
    )
```

```python
import jax
import jax.numpy as jnp
from jax import lax
from jax.sharding import PartitionSpec as P


def shards(states, language, placement, swap_flags, up_weight, down_weight):
    step_count, row_count, model_width = states.shape
    experts = lax.axis_size("expert")
    capacity = max(2, 2 * row_count // experts)
    labels = jnp.arange(experts, dtype=jnp.int32)
    slots_per = step_count * capacity
    steps = jnp.arange(step_count, dtype=jnp.int32)
    placed_hot = placement[:, :, None] == labels[None, None, :]
    flag_at = jnp.sum(jnp.where(placed_hot, swap_flags[None, None, :], 0), axis=2)
    swapped = (steps[:, None] >= 1) & (flag_at == 1)
    route = jnp.where(swapped, (placement + experts // 2) % experts, placement)
    lang_hot = language[:, :, 0][:, :, None] == labels[None, None, :]
    target = jnp.sum(jnp.where(lang_hot, route[:, None, :], 0), axis=2)
    row_ids = jnp.arange(row_count, dtype=jnp.int32)
    same = (target[:, :, None] == target[:, None, :]) & (row_ids[None, None, :] < row_ids[None, :, None])
    position_in = jnp.sum(same.astype(jnp.int32), axis=2)
    slot_id = (target * slots_per + steps[:, None] * capacity + position_in).reshape(-1)
    slot_labels = jnp.arange(experts * slots_per, dtype=jnp.int32)
    select = (slot_id[:, None] == slot_labels[None, :]).astype(jnp.bfloat16)
    rows = states.reshape(step_count * row_count, model_width)
    outgoing = jnp.einsum("rs,rd->sd", select, rows, preferred_element_type=jnp.float32)
    lanes = 128 if model_width % 128 == 0 else model_width
    packed = (experts, slots_per * model_width // lanes, lanes)
    outgoing = outgoing.astype(jnp.bfloat16).reshape(packed)
    arrived = lax.all_to_all(outgoing, "expert", split_axis=0, concat_axis=0, tiled=True)
    flat_rows = arrived.reshape(experts * slots_per, model_width)
    pair = [(0, 1), (1, 0)]
    other_rows = lax.ppermute(flat_rows, "dp", pair)

    def half_ffn(x):
        hidden = jnp.maximum(
            jnp.dot(x, up_weight[0], preferred_element_type=jnp.float32), 0.0
        ).astype(jnp.bfloat16)
        return jnp.dot(hidden, down_weight[0], preferred_element_type=jnp.float32)

    own_part = half_ffn(flat_rows)
    split = other_rows.shape[0] // 2
    sent_back = [
        lax.ppermute(half_ffn(other_rows[:split]), "dp", pair),
        lax.ppermute(half_ffn(other_rows[split:]), "dp", pair),
    ]
    update = own_part + jnp.concatenate(sent_back, axis=0)
    served = update.astype(jnp.bfloat16).reshape(packed)
    returned = lax.all_to_all(served, "expert", split_axis=0, concat_axis=0, tiled=True)
    selected = jnp.dot(
        select,
        returned.reshape(experts * slots_per, model_width),
        preferred_element_type=jnp.float32,
    )
    updated = (rows.astype(jnp.float32) + selected).astype(jnp.bfloat16)
    return updated.reshape(step_count, row_count, model_width)


def solution(mesh):
    placed = (
        P(None, ("dp", "expert"), None),
        P(None, ("dp", "expert"), None),
        P(),
        P(),
        P("expert", None, "dp"),
        P("expert", "dp", None),
    )
    return jax.shard_map(
        shards,
        mesh=mesh,
        in_specs=placed,
        out_specs=P(None, ("dp", "expert"), None),
        check_vma=False,
    )
```

```python
import jax
import jax.numpy as jnp
from jax import lax
from jax.sharding import PartitionSpec as P


def shards(states, language, placement, swap_flags, up_weight, down_weight):
    step_count, row_count, model_width = states.shape
    experts = lax.axis_size("expert")
    capacity = max(2, 2 * row_count // experts)
    labels = jnp.arange(experts, dtype=jnp.int32)
    pair = [(0, 1), (1, 0)]
    other_up = lax.ppermute(up_weight[0], "dp", pair)
    other_down = lax.ppermute(down_weight[0], "dp", pair)
    up_full = jnp.concatenate([up_weight[0], other_up], axis=1)
    down_full = jnp.concatenate([down_weight[0], other_down], axis=0)
    slots_per = step_count * capacity
    steps = jnp.arange(step_count, dtype=jnp.int32)
    placed_hot = placement[:, :, None] == labels[None, None, :]
    flag_at = jnp.sum(jnp.where(placed_hot, swap_flags[None, None, :], 0), axis=2)
    swapped = (steps[:, None] >= 1) & (flag_at == 1)
    route = jnp.where(swapped, (placement + experts // 2) % experts, placement)
    lang_hot = language[:, :, 0][:, :, None] == labels[None, None, :]
    target = jnp.sum(jnp.where(lang_hot, route[:, None, :], 0), axis=2)
    row_ids = jnp.arange(row_count, dtype=jnp.int32)
    same = (target[:, :, None] == target[:, None, :]) & (row_ids[None, None, :] < row_ids[None, :, None])
    position_in = jnp.sum(same.astype(jnp.int32), axis=2)
    slot_id = (target * slots_per + steps[:, None] * capacity + position_in).reshape(-1)
    slot_labels = jnp.arange(experts * slots_per, dtype=jnp.int32)
    select = (slot_id[:, None] == slot_labels[None, :]).astype(jnp.bfloat16)
    rows = states.reshape(step_count * row_count, model_width)
    outgoing = jnp.einsum("rs,rd->sd", select, rows, preferred_element_type=jnp.float32)
    lanes = 128 if model_width % 128 == 0 else model_width
    packed = (experts, slots_per * model_width // lanes, lanes)
    outgoing = outgoing.astype(jnp.bfloat16).reshape(packed)
    arrived = lax.all_to_all(outgoing, "expert", split_axis=0, concat_axis=0, tiled=True)
    flat_rows = arrived.reshape(experts * slots_per, model_width)
    hidden = jnp.maximum(
        jnp.dot(flat_rows, up_full, preferred_element_type=jnp.float32), 0.0
    ).astype(jnp.bfloat16)
    update = jnp.dot(hidden, down_full, preferred_element_type=jnp.float32)
    update = update.astype(jnp.bfloat16).astype(jnp.float32)
    served = (flat_rows.astype(jnp.float32) + update).astype(jnp.bfloat16).reshape(packed)
    returned = lax.all_to_all(served, "expert", split_axis=0, concat_axis=0, tiled=True)
    selected = jnp.dot(
        select,
        returned.reshape(experts * slots_per, model_width),
        preferred_element_type=jnp.float32,
    )
    updated = selected.astype(jnp.bfloat16)
    return updated.reshape(step_count, row_count, model_width)


def solution(mesh):
    placed = (
        P(None, ("dp", "expert"), None),
        P(None, ("dp", "expert"), None),
        P(),
        P(),
        P("expert", None, "dp"),
        P("expert", "dp", None),
    )
    return jax.shard_map(
        shards,
        mesh=mesh,
        in_specs=placed,
        out_specs=P(None, ("dp", "expert"), None),
        check_vma=False,
    )
```

```python
import jax
import jax.numpy as jnp
from jax import lax
from jax.sharding import PartitionSpec as P


def shards(states, language, placement, swap_flags, up_weight, down_weight):
    step_count, row_count, model_width = states.shape
    experts = lax.axis_size("expert")
    capacity = max(2, 2 * row_count // experts)
    labels = jnp.arange(experts, dtype=jnp.int32)
    pair = [(0, 1), (1, 0)]
    other_up = lax.ppermute(up_weight[0], "dp", pair)
    other_down = lax.ppermute(down_weight[0], "dp", pair)
    up_full = jnp.concatenate([up_weight[0], other_up], axis=1)
    down_full = jnp.concatenate([down_weight[0], other_down], axis=0)
    slots_per = step_count * capacity
    steps = jnp.arange(step_count, dtype=jnp.int32)
    placed_hot = placement[:, :, None] == labels[None, None, :]
    flag_at = jnp.sum(jnp.where(placed_hot, swap_flags[None, None, :], 0), axis=2)
    swapped = (steps[:, None] >= 1) & (flag_at == 1)
    route = jnp.where(swapped, (placement + experts // 2) % experts, placement)
    lang_hot = language[:, :, 0][:, :, None] == labels[None, None, :]
    target = jnp.sum(jnp.where(lang_hot, route[:, None, :], 0), axis=2)
    row_ids = jnp.arange(row_count, dtype=jnp.int32)
    same = (target[:, :, None] == target[:, None, :]) & (row_ids[None, None, :] < row_ids[None, :, None])
    position_in = jnp.sum(same.astype(jnp.int32), axis=2)
    slot_id = (target * slots_per + steps[:, None] * capacity + position_in).reshape(-1)
    slot_labels = jnp.arange(experts * slots_per, dtype=jnp.int32)
    select = (slot_id[:, None] == slot_labels[None, :]).astype(jnp.bfloat16)
    rows = states.reshape(step_count * row_count, model_width)
    gather = (slot_labels[:, None] == slot_id[None, :]).astype(jnp.bfloat16)
    outgoing = jnp.dot(gather, rows, preferred_element_type=jnp.float32)
    lanes = 128 if model_width % 128 == 0 else model_width
    packed = (experts, slots_per * model_width // lanes, lanes)
    outgoing = outgoing.astype(jnp.bfloat16).reshape(packed)
    arrived = lax.all_to_all(outgoing, "expert", split_axis=0, concat_axis=0, tiled=True)
    flat_rows = arrived.reshape(experts * slots_per, model_width)
    hidden = jnp.maximum(
        jnp.dot(flat_rows, up_full, preferred_element_type=jnp.float32), 0.0
    ).astype(jnp.bfloat16)
    update = jnp.dot(hidden, down_full, preferred_element_type=jnp.float32)
    served = update.astype(jnp.bfloat16).reshape(packed)
    returned = lax.all_to_all(served, "expert", split_axis=0, concat_axis=0, tiled=True)
    selected = jnp.dot(
        select,
        returned.reshape(experts * slots_per, model_width),
        preferred_element_type=jnp.float32,
    )
    updated = (rows.astype(jnp.float32) + selected).astype(jnp.bfloat16)
    return updated.reshape(step_count, row_count, model_width)


def solution(mesh):
    placed = (
        P(None, ("dp", "expert"), None),
        P(None, ("dp", "expert"), None),
        P(),
        P(),
        P("expert", None, "dp"),
        P("expert", "dp", None),
    )
    return jax.shard_map(
        shards,
        mesh=mesh,
        in_specs=placed,
        out_specs=P(None, ("dp", "expert"), None),
        check_vma=False,
    )
```

```python
import jax
import jax.numpy as jnp
from jax import lax
from jax.sharding import PartitionSpec as P


def shards(states, language, placement, swap_flags, up_weight, down_weight):
    step_count, row_count, model_width = states.shape
    experts = lax.axis_size("expert")
    capacity = max(2, 2 * row_count // experts)
    labels = jnp.arange(experts, dtype=jnp.int32)
    pair = [(0, 1), (1, 0)]
    other_up = lax.ppermute(up_weight[0], "dp", pair)
    other_down = lax.ppermute(down_weight[0], "dp", pair)
    slots_per = step_count * capacity
    steps = jnp.arange(step_count, dtype=jnp.int32)
    placed_hot = placement[:, :, None] == labels[None, None, :]
    flag_at = jnp.sum(jnp.where(placed_hot, swap_flags[None, None, :], 0), axis=2)
    swapped = (steps[:, None] >= 1) & (flag_at == 1)
    route = jnp.where(swapped, (placement + experts // 2) % experts, placement)
    lang_hot = language[:, :, 0][:, :, None] == labels[None, None, :]
    target = jnp.sum(jnp.where(lang_hot, route[:, None, :], 0), axis=2)
    row_ids = jnp.arange(row_count, dtype=jnp.int32)
    same = (target[:, :, None] == target[:, None, :]) & (row_ids[None, None, :] < row_ids[None, :, None])
    position_in = jnp.sum(same.astype(jnp.int32), axis=2)
    slot_id = (target * slots_per + steps[:, None] * capacity + position_in).reshape(-1)
    slot_labels = jnp.arange(experts * slots_per, dtype=jnp.int32)
    select = (slot_id[:, None] == slot_labels[None, :]).astype(jnp.bfloat16)
    rows = states.reshape(step_count * row_count, model_width)
    outgoing = jnp.einsum("rs,rd->sd", select, rows, preferred_element_type=jnp.float32)
    lanes = 128 if model_width % 128 == 0 else model_width
    packed = (experts, slots_per * model_width // lanes, lanes)
    outgoing = outgoing.astype(jnp.bfloat16).reshape(packed)
    arrived = lax.all_to_all(outgoing, "expert", split_axis=0, concat_axis=0, tiled=True)
    flat_rows = arrived.reshape(experts * slots_per, model_width)
    def half_ffn(up_half, down_half):
        hidden = jnp.maximum(
            jnp.dot(flat_rows, up_half, preferred_element_type=jnp.float32), 0.0
        ).astype(jnp.bfloat16)
        return jnp.dot(hidden, down_half, preferred_element_type=jnp.float32)

    update = half_ffn(up_weight[0], down_weight[0]) + half_ffn(other_up, other_down)
    served = update.astype(jnp.bfloat16).reshape(packed)
    returned = lax.all_to_all(served, "expert", split_axis=0, concat_axis=0, tiled=True)
    selected = jnp.dot(
        select,
        returned.reshape(experts * slots_per, model_width),
        preferred_element_type=jnp.float32,
    )
    updated = (rows.astype(jnp.float32) + selected).astype(jnp.bfloat16)
    return updated.reshape(step_count, row_count, model_width)


def solution(mesh):
    placed = (
        P(None, ("dp", "expert"), None),
        P(None, ("dp", "expert"), None),
        P(),
        P(),
        P("expert", None, "dp"),
        P("expert", "dp", None),
    )
    return jax.shard_map(
        shards,
        mesh=mesh,
        in_specs=placed,
        out_specs=P(None, ("dp", "expert"), None),
        check_vma=False,
    )
```

```python
import jax
import jax.numpy as jnp
from jax import lax
from jax.sharding import PartitionSpec as P


def shards(states, language, placement, swap_flags, up_weight, down_weight):
    step_count, row_count, model_width = states.shape
    experts = lax.axis_size("expert")
    capacity = max(2, 2 * row_count // experts)
    labels = jnp.arange(experts, dtype=jnp.int32)
    pair = [(0, 1), (1, 0)]
    other_up = lax.ppermute(up_weight[0], "dp", pair)
    other_down = lax.ppermute(down_weight[0], "dp", pair)
    up_full = jnp.concatenate([up_weight[0], other_up], axis=1)
    down_full = jnp.concatenate([down_weight[0], other_down], axis=0)
    slots_per = step_count * capacity
    steps = jnp.arange(step_count, dtype=jnp.int32)
    placed_hot = placement[:, :, None] == labels[None, None, :]
    flag_at = jnp.sum(jnp.where(placed_hot, swap_flags[None, None, :], 0), axis=2)
    swapped = (steps[:, None] >= 1) & (flag_at == 1)
    route = jnp.where(swapped, (placement + experts // 2) % experts, placement)
    lang_hot = language[:, :, 0][:, :, None] == labels[None, None, :]
    target = jnp.sum(jnp.where(lang_hot, route[:, None, :], 0), axis=2)
    row_ids = jnp.arange(row_count, dtype=jnp.int32)
    same = (target[:, :, None] == target[:, None, :]) & (row_ids[None, None, :] < row_ids[None, :, None])
    position_in = jnp.sum(same.astype(jnp.int32), axis=2)
    slot_id = (target * slots_per + steps[:, None] * capacity + position_in).reshape(-1)
    slot_labels = jnp.arange(experts * slots_per, dtype=jnp.int32)
    select = (slot_id[:, None] == slot_labels[None, :]).astype(jnp.bfloat16)
    rows = states.reshape(step_count * row_count, model_width)
    outgoing = jnp.einsum("rs,rd->sd", select, rows, preferred_element_type=jnp.float32)
    lanes = 128 if model_width % 128 == 0 else model_width
    packed = (experts, slots_per * model_width // lanes, lanes)
    outgoing = outgoing.astype(jnp.bfloat16).reshape(packed)
    arrived = lax.all_to_all(outgoing, "expert", split_axis=0, concat_axis=0, tiled=True)
    flat_rows = arrived.reshape(experts * slots_per, model_width)
    hidden = jnp.maximum(
        jnp.einsum(
            "dcl,clh->dh",
            arrived.reshape(experts * slots_per, model_width // lanes, lanes),
            up_full.reshape(model_width // lanes, lanes, up_full.shape[1]),
            preferred_element_type=jnp.float32,
        ), 0.0
    ).astype(jnp.bfloat16)
    update = jnp.dot(hidden, down_full, preferred_element_type=jnp.float32)
    served = update.astype(jnp.bfloat16).reshape(packed)
    returned = lax.all_to_all(served, "expert", split_axis=0, concat_axis=0, tiled=True)
    selected = jnp.dot(
        select,
        returned.reshape(experts * slots_per, model_width),
        preferred_element_type=jnp.float32,
    )
    updated = (rows.astype(jnp.float32) + selected).astype(jnp.bfloat16)
    return updated.reshape(step_count, row_count, model_width)


def solution(mesh):
    placed = (
        P(None, ("dp", "expert"), None),
        P(None, ("dp", "expert"), None),
        P(),
        P(),
        P("expert", None, "dp"),
        P("expert", "dp", None),
    )
    return jax.shard_map(
        shards,
        mesh=mesh,
        in_specs=placed,
        out_specs=P(None, ("dp", "expert"), None),
        check_vma=False,
    )
```

```python
import jax
import jax.numpy as jnp
from jax import lax
from jax.sharding import PartitionSpec as P


def shards(states, language, placement, swap_flags, up_weight, down_weight):
    step_count, row_count, model_width = states.shape
    experts = lax.axis_size("expert")
    capacity = max(2, 2 * row_count // experts)
    labels = jnp.arange(experts, dtype=jnp.int32)
    pair = [(0, 1), (1, 0)]
    other_up = lax.ppermute(up_weight[0], "dp", pair)
    other_down = lax.ppermute(down_weight[0], "dp", pair)
    up_full = jnp.concatenate([up_weight[0], other_up], axis=1)
    down_full = jnp.concatenate([down_weight[0], other_down], axis=0)
    slots_per = step_count * capacity
    steps = jnp.arange(step_count, dtype=jnp.int32)
    placed_hot = placement[:, :, None] == labels[None, None, :]
    flag_at = jnp.sum(jnp.where(placed_hot, swap_flags[None, None, :], 0), axis=2)
    swapped = (steps[:, None] >= 1) & (flag_at == 1)
    route = jnp.where(swapped, (placement + experts // 2) % experts, placement)
    lang_hot = language[:, :, 0][:, :, None] == labels[None, None, :]
    target = jnp.sum(jnp.where(lang_hot, route[:, None, :], 0), axis=2)
    row_ids = jnp.arange(row_count, dtype=jnp.int32)
    same = (target[:, :, None] == target[:, None, :]) & (row_ids[None, None, :] < row_ids[None, :, None])
    position_in = jnp.sum(same.astype(jnp.int32), axis=2)
    slot_id = (target * slots_per + steps[:, None] * capacity + position_in).reshape(-1)
    slot_labels = jnp.arange(experts * slots_per, dtype=jnp.int32)
    select = (slot_id[:, None] == slot_labels[None, :]).astype(jnp.bfloat16)
    rows = states.reshape(step_count * row_count, model_width)
    outgoing = jnp.einsum("rs,rd->sd", select, rows, preferred_element_type=jnp.float32)
    lanes = 128 if model_width % 128 == 0 else model_width
    packed = (experts, slots_per * model_width // lanes, lanes)
    outgoing = outgoing.astype(jnp.bfloat16).reshape(packed)
    arrived = lax.all_to_all(outgoing, "expert", split_axis=0, concat_axis=0, tiled=True)
    flat_rows = arrived.reshape(experts * slots_per, model_width)
    hidden = jnp.maximum(
        jnp.einsum(
            "dcl,clh->dh",
            arrived.reshape(experts * slots_per, model_width // lanes, lanes),
            up_full.reshape(model_width // lanes, lanes, up_full.shape[1]),
            preferred_element_type=jnp.float32,
        ), 0.0
    ).astype(jnp.bfloat16)
    update = jnp.dot(hidden, down_full, preferred_element_type=jnp.float32)
    served = update.astype(jnp.bfloat16).reshape(packed)
    returned = lax.all_to_all(served, "expert", split_axis=0, concat_axis=0, tiled=True)
    selected = jnp.einsum(
        "rs,scl->rcl",
        select,
        returned.reshape(experts * slots_per, model_width // lanes, lanes),
        preferred_element_type=jnp.float32,
    ).reshape(step_count * row_count, model_width)
    updated = (rows.astype(jnp.float32) + selected).astype(jnp.bfloat16)
    return updated.reshape(step_count, row_count, model_width)


def solution(mesh):
    placed = (
        P(None, ("dp", "expert"), None),
        P(None, ("dp", "expert"), None),
        P(),
        P(),
        P("expert", None, "dp"),
        P("expert", "dp", None),
    )
    return jax.shard_map(
        shards,
        mesh=mesh,
        in_specs=placed,
        out_specs=P(None, ("dp", "expert"), None),
        check_vma=False,
    )
```
